512 devices in a mesh: expert: 32 (over x, y, core), replica: 16 (over z).
Axes of the slice: x: 4, y: 4, z: 16, core: 2. Of those that a mesh axis runs over, the one named last changes fastest.
Arguments:
- tokens: bfloat16 [65536, 2560], P(('expert', 'replica')), may hold values from -6 to 6
- cotangent: bfloat16 [65536, 2560], P(('expert', 'replica')), may hold values from -4 to 4
- partner: int32 [65536, 1], P(('expert', 'replica')), may hold values from 0 to 31; in each aligned block of 128 rows (0 to 127, 128 to 255, ...) at most 5 rows name the same one
- combine: int32 [65536, 2], P(('expert', 'replica')), may hold values from 1 to 8
- counts: int32 [512], P(('expert', 'replica')), may hold values from 32 to 128, as said below
- w_gate: bfloat16 [32, 2560, 768], P('expert', 'replica'), may hold values from -0.125 to 0.125
- w_up: bfloat16 [32, 2560, 768], P('expert', 'replica'), may hold values from -0.125 to 0.125
- w_down: bfloat16 [32, 768, 2560], P('expert', 'replica'), may hold values from -0.21875 to 0.21875
Outputs:
- token_grad: bfloat16 [65536, 2560], P(('expert', 'replica'))
- grad_down: bfloat16 [32, 768, 2560], P('expert', 'replica')
The draws below stay inside these ranges and needn't reach their ends.
Inputs may be any that keep to these rules, and one draw needn't show every extreme that they name: `partner`: within the 128 rows of one device no expert index is named by more than 5 rows, and some device names one exactly 5 times. `counts`: some device has all 128 slots real.
All inputs are finite; a program needn't handle non-finite values.
Results may differ from the reference program's by a relative error of at most 0.017.
Values may be sent and summed in bfloat16 or wider, within the bound.
No kernel may reach another device: no remote copies, remote signals or barrier semaphores. Data moves between devices by JAX's collectives and lax.ppermute only.
A program may use at most 64 MiB of HBM per device.

```python
import math
import jax
import jax.numpy as jnp
import numpy as np
from jax import lax

D = 2560
H = 768
TOK_DEV = 128
CAP = 5
EXPERTS = 32
SHARDS = 512
TOKENS = 65536
N_EXPERT = 32
N_REPLICA = 16


def draw_counts(key, part):
    base = jax.random.randint(key, (SHARDS,), TOK_DEV // 4, TOK_DEV + 1)
    chosen = jax.random.randint(jax.random.fold_in(key, 7), (), 0, SHARDS)
    return jnp.where(jnp.arange(SHARDS) == chosen, TOK_DEV, base).astype(jnp.int32)


def touch_ends(entries, rng, low, high):
    index_at = [jax.random.randint(jax.random.fold_in(rng, axis), (), 0, length) for axis, length in enumerate(entries.shape)]
    main_axis = entries.shape.index(max(entries.shape))
    next_to = index_at[:main_axis] + [(index_at[main_axis] + 1) % entries.shape[main_axis]] + index_at[main_axis + 1:]
    return entries.at[tuple(index_at)].set(low).at[tuple(next_to)].set(high)


def level_of(own_key, shape, cuts, low, top_value):
    factor_of, own = 1.0, jax.random.fold_in(own_key, 6)
    for dim, parts in cuts:
        steps = jnp.exp(jax.random.uniform(jax.random.fold_in(own, dim), (parts,), jnp.float32, low / len(cuts), top_value / len(cuts)))
        factor_of = factor_of * jnp.repeat(steps, shape[dim] // parts).reshape([-1 if axis == dim else 1 for axis in range(len(shape))])
    return factor_of


def shared_out(rng, own, number, rows, number_of, top, limit, slope):
    order = jax.random.permutation(rng, number_of)
    packed, usual = shares(number_of, rows * top, limit, slope, True), shares(number_of, rows * top, limit, slope, False)
    places = jnp.arange(number_of)

    def named(tallies, rotation):
        used = int((tallies > 0).sum())
        fixed = max(1, used // 4)
        passed = fixed + (places - fixed + rotation * (used - fixed)) % max(1, number_of - fixed)
        return jnp.zeros((number_of,), jnp.int32).at[order[jnp.where(places < fixed, places, passed)]].set(jnp.asarray(tallies, jnp.int32))

    tallies = jnp.where(number % 4 == 0, named(packed, number // 4), named(usual, number - number // 4 - 1))
    mixed = jax.random.permutation(jax.random.fold_in(own, 3), number_of)
    donor, receiver = mixed[0:number_of // 2 * 2:2], mixed[1:number_of // 2 * 2:2]
    margin = jnp.minimum(tallies[donor] - 1, limit - tallies[receiver]) // 2
    margin = jnp.where((donor == order[0]) | (receiver == order[0]) | (tallies[receiver] == 0), 0, jnp.maximum(margin, 0))
    passed = jax.random.randint(jax.random.fold_in(own, 4), (number_of // 2,), 0, 1 << 20) % (margin + 1)
    tallies = tallies.at[donor].add(-passed).at[receiver].add(passed)
    items = jnp.searchsorted(jnp.cumsum(tallies), jnp.arange(rows * top), side="right").astype(jnp.int32)
    table = items.reshape(top, rows).T
    table = table[jax.random.permutation(jax.random.fold_in(own, 1), rows)]
    rotation = jax.random.randint(jax.random.fold_in(own, 2), (rows, 1), 0, top)
    return jnp.take_along_axis(table, (jnp.arange(top)[None, :] + rotation) % top, axis=1)


def shares(amount, total, bound, lean, full):
    loads = [(1 << 20) // math.isqrt(standing ** lean) + 1 for standing in range(1, amount + 1)]
    largest = bound if full else min(bound, max(-(-total // amount), total * loads[0] // sum(loads)))
    least = 1 if total - largest >= amount - 1 else 0
    given, surplus = [largest] + [least] * (amount - 1), total - largest - least * (amount - 1)
    while surplus > 0:
        candidates = [i for i in range(1, amount) if given[i] < largest] or [i for i in range(1, amount) if given[i] < bound]
        whole, remaining = sum([loads[i] for i in candidates]), surplus
        for i in candidates:
            extra = min(bound - given[i], max(1, remaining * loads[i] // whole), surplus)
            given[i] = given[i] + extra
            surplus = surplus - extra
    return np.array(given)


def gaussian(own_key, shape, scale, bound, shards=(), kind=jnp.bfloat16):
    drawn = jax.random.normal(own_key, shape, jnp.float32) * scale
    if len(shards) > 0:
        drawn = level_of(own_key, shape, shards, -0.22, 0.18) * drawn
    return jnp.clip(drawn, min=-bound, max=bound).astype(kind)


def setup_inputs(seed: int = 0) -> dict:
    key_list = jax.random.split(jax.random.key(seed), 9)
    tokens = gaussian(key_list[0], (TOKENS, D), 1.0, 6.0, ((0, 512),))
    cotangent = gaussian(key_list[1], (TOKENS, D), 0.5, 4.0, ((0, 512),))
    partner_keys = jax.random.split(jax.random.fold_in(key_list[2], 1), TOKENS // TOK_DEV)
    partner_turns = jax.random.permutation(jax.random.fold_in(key_list[2], 3), TOKENS // TOK_DEV)
    partner = jax.vmap(lambda own, number: shared_out(jax.random.fold_in(key_list[2], 2), own, number, TOK_DEV, N_EXPERT, 1, CAP, 2))(partner_keys, partner_turns).reshape((TOKENS, 1))
    combine = touch_ends(jax.random.randint(key_list[3], (TOKENS, 2), 1, 9), jax.random.fold_in(key_list[3], 1), 1, 8).astype(jnp.int32)
    counts = draw_counts(jax.random.fold_in(key_list[8], 71), 0)
    w_gate = gaussian(key_list[5], (EXPERTS, D, H), D ** -0.5, 0.125, ((0, 32), (1, 16)))
    w_up = gaussian(key_list[6], (EXPERTS, D, H), D ** -0.5, 0.125, ((0, 32), (1, 16)))
    w_down = gaussian(key_list[7], (EXPERTS, H, D), H ** -0.5, 0.21875, ((0, 32), (1, 16)))
    return dict(tokens=tokens, cotangent=cotangent, partner=partner, combine=combine, counts=counts, w_gate=w_gate, w_up=w_up, w_down=w_down)


def expert_backward(inputs, upstream, gate_w, up_w, down_w):
    gate_act = jnp.dot(inputs, gate_w, preferred_element_type=jnp.float32)
    up_act = jnp.dot(inputs, up_w, preferred_element_type=jnp.float32)
    sigmoid_gate = jax.nn.sigmoid(gate_act)
    swish_gate = gate_act * sigmoid_gate
    hidden = (swish_gate * up_act).astype(jnp.bfloat16)
    hidden_grad = jnp.dot(upstream, down_w.T, preferred_element_type=jnp.float32)
    gate_grad = (hidden_grad * up_act * sigmoid_gate * (1.0 + gate_act * (1.0 - sigmoid_gate))).astype(jnp.bfloat16)
    up_grad = (hidden_grad * swish_gate).astype(jnp.bfloat16)
    input_grad = jnp.dot(gate_grad, gate_w.T, preferred_element_type=jnp.float32) + jnp.dot(up_grad, up_w.T, preferred_element_type=jnp.float32)
    return hidden, input_grad


def reference(tokens, cotangent, partner, combine, counts, w_gate, w_up, w_down):
    token_ids = jnp.arange(TOKENS, dtype=jnp.int32)
    device_ids = token_ids // TOK_DEV
    valid_rows = (token_ids % TOK_DEV) < counts[device_ids]
    weights = combine.astype(jnp.float32)
    weight_sum = weights[:, 0] + weights[:, 1]
    share_home = jnp.where(valid_rows, weights[:, 0] / weight_sum, 0.0)
    share_away = jnp.where(valid_rows, weights[:, 1] / weight_sum, 0.0)
    upstream = cotangent.astype(jnp.float32)
    q_home = (upstream * share_home[:, None]).astype(jnp.bfloat16)
    q_away = (upstream * share_away[:, None]).astype(jnp.bfloat16)
    target = partner[:, 0].astype(jnp.int32)
    onehot_rows = (target.reshape(SHARDS, TOK_DEV)[:, :, None] == jnp.arange(N_EXPERT, dtype=jnp.int32)[None, None, :]).astype(jnp.int32)
    rank_within = jnp.sum((jnp.cumsum(onehot_rows, axis=1) - onehot_rows) * onehot_rows, axis=2).reshape(TOKENS).astype(jnp.int32)
    slot_index = (device_ids * CAP + rank_within).astype(jnp.int32)
    slot_table = jnp.full((N_EXPERT, SHARDS * CAP), TOKENS, dtype=jnp.int32).at[target, slot_index].set(token_ids)
    padded_x = jnp.concatenate([tokens, jnp.zeros((1, D), tokens.dtype)], axis=0)
    padded_q = jnp.concatenate([q_away, jnp.zeros((1, D), q_away.dtype)], axis=0)
    home_x = tokens.reshape(N_EXPERT, N_REPLICA * TOK_DEV, D)
    home_q = q_home.reshape(N_EXPERT, N_REPLICA * TOK_DEV, D)

    def per_expert(operands):
        x_home, q_here, slots, gate_w, up_w, down_w = operands
        hidden_home, grad_home = expert_backward(x_home, q_here, gate_w, up_w, down_w)
        x_away = jnp.take(padded_x, slots, axis=0)
        q_there = jnp.take(padded_q, slots, axis=0)
        hidden_away, grad_away = expert_backward(x_away, q_there, gate_w, up_w, down_w)
        part_home = jnp.einsum("rth,rtd->rhd", hidden_home.reshape(N_REPLICA, TOK_DEV, H).astype(jnp.float32), q_here.reshape(N_REPLICA, TOK_DEV, D).astype(jnp.float32))
        part_away = jnp.einsum("srch,srcd->rhd", hidden_away.reshape(N_EXPERT, N_REPLICA, CAP, H).astype(jnp.float32), q_there.reshape(N_EXPERT, N_REPLICA, CAP, D).astype(jnp.float32))
        partial_grad = lax.optimization_barrier((part_home + part_away).astype(jnp.bfloat16))
        grad_down = jnp.sum(partial_grad.astype(jnp.float32), axis=0).astype(jnp.bfloat16)
        return grad_home, grad_away.astype(jnp.bfloat16), grad_down

    grad_home_all, grad_away_all, grad_down = lax.map(per_expert, (home_x, home_q, slot_table, w_gate, w_up, w_down))
    grad_home_flat = grad_home_all.reshape(TOKENS, D)
    grad_away_flat = grad_away_all[target, slot_index]
    token_grad = (grad_home_flat + grad_away_flat.astype(jnp.float32)).astype(jnp.bfloat16)
    return token_grad, grad_down
```

```python
import jax
import jax.numpy as jnp
from jax import lax
from jax.sharding import PartitionSpec as P


def against_rows(left, matrix):
    return lax.dot_general(
        left, matrix, (((1,), (1,)), ((), ())), preferred_element_type=jnp.float32
    )


def expert_backward(inputs, upstream, gate_w, up_w, down_w):
    gate_act = jnp.dot(inputs, gate_w, preferred_element_type=jnp.float32)
    up_act = jnp.dot(inputs, up_w, preferred_element_type=jnp.float32)
    sigmoid_gate = jax.nn.sigmoid(gate_act)
    swish_gate = gate_act * sigmoid_gate
    hidden = (swish_gate * up_act).astype(jnp.bfloat16)
    hidden_grad = against_rows(upstream, down_w)
    gate_grad = (
        hidden_grad * up_act * sigmoid_gate * (1.0 + gate_act * (1.0 - sigmoid_gate))
    ).astype(jnp.bfloat16)
    up_grad = (hidden_grad * swish_gate).astype(jnp.bfloat16)
    input_grad = against_rows(gate_grad, gate_w) + against_rows(up_grad, up_w)
    return (hidden, input_grad)


def ring_gather(parts, axis):
    n = lax.axis_size(axis)
    idx = lax.axis_index(axis)
    right = [(i, (i + 1) % n) for i in range(n)]
    left = [(i, (i - 1) % n) for i in range(n)]
    fulls = [jnp.zeros((n,) + p.shape, p.dtype) for p in parts]

    def put(fulls, pieces, d):
        pos = (idx + d) % n
        return [lax.dynamic_update_index_in_dim(f, p, pos, 0) for f, p in zip(fulls, pieces)]

    fulls = put(fulls, parts, 0)
    r, l = list(parts), list(parts)
    half = n // 2
    steps = half if n % 2 == 1 else half - 1
    for k in range(1, steps + 1):
        r = [lax.ppermute(p, axis, right) for p in r]
        l = [lax.ppermute(p, axis, left) for p in l]
        fulls = put(fulls, r, -k)
        fulls = put(fulls, l, k)
    if n % 2 == 0 and n > 1:
        cut = [p.shape[-1] // 2 for p in parts]
        rh = [lax.ppermute(p[..., :c], axis, right) for p, c in zip(r, cut)]
        lh = [lax.ppermute(p[..., c:], axis, left) for p, c in zip(l, cut)]
        last = [jnp.concatenate([a, b], axis=-1) for a, b in zip(rh, lh)]
        fulls = put(fulls, last, half)
    return fulls


def ring_reduce_scatter(blocks, axis):
    n = lax.axis_size(axis)
    idx = lax.axis_index(axis)
    right = [(i, (i + 1) % n) for i in range(n)]
    left = [(i, (i - 1) % n) for i in range(n)]

    def blk(k):
        return lax.dynamic_index_in_dim(blocks, (idx + k) % n, 0, keepdims=False)

    n_right = n // 2
    n_left = n - 1 - n_right
    out = blk(0)
    recv_r = recv_l = None
    for s in range(1, max(n_right, n_left) + 1):
        if s <= n_right:
            mine = blk(n_right + 1 - s)
            acc = mine if recv_r is None else recv_r.astype(jnp.float32) + mine
            recv_r = lax.ppermute(acc.astype(jnp.bfloat16), axis, right)
        if s <= n_left:
            mine = blk(-(n_left + 1 - s))
            acc = mine if recv_l is None else recv_l.astype(jnp.float32) + mine
            recv_l = lax.ppermute(acc.astype(jnp.bfloat16), axis, left)
    if recv_r is not None:
        out = out + recv_r.astype(jnp.float32)
    if recv_l is not None:
        out = out + recv_l.astype(jnp.float32)
    return out


def local(tokens, cotangent, partner, combine, counts, w_gate, w_up, w_down):
    tok_rows = tokens.shape[0]
    width = tokens.shape[1]
    expert_count = lax.axis_size("expert")
    capacity = max(2, (5 * tok_rows // 4 + expert_count - 1) // expert_count)
    positions = jnp.arange(tok_rows, dtype=jnp.int32)
    valid_rows = positions < counts[0]
    weights = combine.astype(jnp.float32)
    weight_sum = weights[:, 0] + weights[:, 1]
    share_home = jnp.where(valid_rows, weights[:, 0] / weight_sum, 0.0)
    share_away = jnp.where(valid_rows, weights[:, 1] / weight_sum, 0.0)
    upstream = cotangent.astype(jnp.float32)
    q_home = (upstream * share_home[:, None]).astype(jnp.bfloat16)
    q_away = (upstream * share_away[:, None]).astype(jnp.bfloat16)
    gate_full, up_full, down_full = ring_gather([w_gate[0], w_up[0], w_down[0]], "replica")
    gate_w = gate_full.reshape(-1, gate_full.shape[2])
    up_w = up_full.reshape(-1, up_full.shape[2])
    down_w = down_full.reshape(-1, down_full.shape[2])
    target = partner[:, 0]
    onehot_rows = (target[:, None] == jnp.arange(expert_count, dtype=jnp.int32)[None, :]).astype(
        jnp.int32
    )
    rank_within = jnp.sum((jnp.cumsum(onehot_rows, axis=0) - onehot_rows) * onehot_rows, axis=1)
    destination = target * capacity + rank_within
    placing = (
        jnp.arange(expert_count * capacity, dtype=jnp.int32)[:, None] == destination[None, :]
    ).astype(jnp.bfloat16)
    send_x = (
        jnp.dot(placing, tokens, preferred_element_type=jnp.float32)
        .astype(jnp.bfloat16)
        .reshape(expert_count, capacity, width)
    )
    send_q = (
        jnp.dot(placing, q_away, preferred_element_type=jnp.float32)
        .astype(jnp.bfloat16)
        .reshape(expert_count, capacity, width)
    )
    hidden_home, grad_home = expert_backward(tokens, q_home, gate_w, up_w, down_w)
    x_there = lax.all_to_all(send_x, "expert", split_axis=0, concat_axis=0, tiled=True)
    q_there = lax.all_to_all(send_q, "expert", split_axis=0, concat_axis=0, tiled=True)
    item_count = x_there.shape[1]
    hidden_there, grad_there = expert_backward(
        x_there.reshape(-1, width), q_there.reshape(-1, width), gate_w, up_w, down_w
    )
    returned = lax.all_to_all(
        grad_there.astype(jnp.bfloat16).reshape(expert_count, item_count, width),
        "expert",
        split_axis=0,
        concat_axis=0,
        tiled=True,
    )
    returned, hidden_away, q_there = (
        returned,
        hidden_there.reshape(expert_count, item_count, -1),
        q_there,
    )
    contract = (((0,), (0,)), ((), ()))
    flat_returned = returned.reshape(expert_count * capacity, width)
    grad_away = lax.dot_general(
        placing, flat_returned, contract, preferred_element_type=jnp.float32
    )
    token_grad = (grad_home + grad_away).astype(jnp.bfloat16)
    flat_hidden = hidden_away.reshape(expert_count * capacity, -1)
    flat_q = q_there.reshape(expert_count * capacity, width)
    partial = lax.dot_general(
        hidden_home, q_home, contract, preferred_element_type=jnp.float32
    ) + lax.dot_general(flat_hidden, flat_q, contract, preferred_element_type=jnp.float32)
    n_rep = lax.axis_size("replica")
    grad_down = ring_reduce_scatter(
        partial.reshape(n_rep, -1, partial.shape[1]), "replica"
    ).astype(jnp.bfloat16)
    return (token_grad, grad_down[None])


def solution(mesh):
    placed = (
        P(("expert", "replica"), None),
        P(("expert", "replica"), None),
        P(("expert", "replica"), None),
        P(("expert", "replica"), None),
        P(("expert", "replica")),
        P("expert", "replica", None),
        P("expert", "replica", None),
        P("expert", "replica", None),
    )
    return jax.shard_map(
        local,
        mesh=mesh,
        in_specs=placed,
        out_specs=(P(("expert", "replica"), None), P("expert", "replica", None)),
        check_vma=False,
    )
```

```python
import jax
import jax.numpy as jnp
from jax import lax
from jax.sharding import PartitionSpec as P


def against_rows(left, matrix):
    return lax.dot_general(
        left, matrix, (((1,), (1,)), ((), ())), preferred_element_type=jnp.float32
    )


def expert_backward(inputs, upstream, gate_w, up_w, down_w):
    gate_act = jnp.dot(inputs, gate_w, preferred_element_type=jnp.float32)
    up_act = jnp.dot(inputs, up_w, preferred_element_type=jnp.float32)
    sigmoid_gate = jax.nn.sigmoid(gate_act)
    swish_gate = gate_act * sigmoid_gate
    hidden = (swish_gate * up_act).astype(jnp.bfloat16)
    hidden_grad = against_rows(upstream, down_w)
    gate_grad = (
        hidden_grad * up_act * sigmoid_gate * (1.0 + gate_act * (1.0 - sigmoid_gate))
    ).astype(jnp.bfloat16)
    up_grad = (hidden_grad * swish_gate).astype(jnp.bfloat16)
    input_grad = against_rows(gate_grad, gate_w) + against_rows(up_grad, up_w)
    return (hidden, input_grad)


def ring_plan():
    n_exp = lax.axis_size("expert")
    n = lax.axis_size("replica")
    perm = []
    for e in range(n_exp):
        step = 1 if e % 2 == 0 else n - 1
        perm += [(e * n + r, e * n + (r + step) % n) for r in range(n)]
    r = lax.axis_index("replica")
    toward = 1 - 2 * (lax.axis_index("expert") % 2)
    return n, r, toward, perm


def ring_gather(piece):
    n, r, toward, perm = ring_plan()
    pieces = [piece]
    for _ in range(n - 1):
        pieces.append(lax.ppermute(pieces[-1], ("expert", "replica"), perm))
    stacked = jnp.stack(pieces)
    order = (toward * (r - jnp.arange(n, dtype=jnp.int32))) % n
    return jnp.take(stacked, order, axis=0)


def ring_reduce_scatter(blocks):
    n, r, toward, perm = ring_plan()

    def blk(k):
        return lax.dynamic_index_in_dim(blocks, k % n, 0, keepdims=False)

    recv = None
    for s in range(1, n):
        mine = blk(r - s * toward)
        acc = mine if recv is None else recv.astype(jnp.float32) + mine
        recv = lax.ppermute(acc.astype(jnp.bfloat16), ("expert", "replica"), perm)
    out = blk(r)
    if recv is not None:
        out = out + recv.astype(jnp.float32)
    return out


def local(tokens, cotangent, partner, combine, counts, w_gate, w_up, w_down):
    tok_rows = tokens.shape[0]
    width = tokens.shape[1]
    expert_count = lax.axis_size("expert")
    capacity = max(2, (5 * tok_rows // 4 + expert_count - 1) // expert_count)
    positions = jnp.arange(tok_rows, dtype=jnp.int32)
    valid_rows = positions < counts[0]
    weights = combine.astype(jnp.float32)
    weight_sum = weights[:, 0] + weights[:, 1]
    share_home = jnp.where(valid_rows, weights[:, 0] / weight_sum, 0.0)
    share_away = jnp.where(valid_rows, weights[:, 1] / weight_sum, 0.0)
    upstream = cotangent.astype(jnp.float32)
    q_home = (upstream * share_home[:, None]).astype(jnp.bfloat16)
    q_away = (upstream * share_away[:, None]).astype(jnp.bfloat16)
    shard_rows, hidden_units = w_gate.shape[1], w_gate.shape[2]
    full = ring_gather(
        jnp.stack([w_gate[0], w_up[0], w_down[0].reshape(shard_rows, hidden_units)])
    )
    gate_w = full[:, 0].reshape(-1, hidden_units)
    up_w = full[:, 1].reshape(-1, hidden_units)
    down_w = full[:, 2].reshape(-1, w_down.shape[1], w_down.shape[2]).reshape(-1, w_down.shape[2])
    target = partner[:, 0]
    onehot_rows = (target[:, None] == jnp.arange(expert_count, dtype=jnp.int32)[None, :]).astype(
        jnp.int32
    )
    rank_within = jnp.sum((jnp.cumsum(onehot_rows, axis=0) - onehot_rows) * onehot_rows, axis=1)
    destination = target * capacity + rank_within
    placing = (
        jnp.arange(expert_count * capacity, dtype=jnp.int32)[:, None] == destination[None, :]
    ).astype(jnp.bfloat16)
    send_x = (
        jnp.dot(placing, tokens, preferred_element_type=jnp.float32)
        .astype(jnp.bfloat16)
        .reshape(expert_count, capacity, width)
    )
    send_q = (
        jnp.dot(placing, q_away, preferred_element_type=jnp.float32)
        .astype(jnp.bfloat16)
        .reshape(expert_count, capacity, width)
    )
    hidden_home, grad_home = expert_backward(tokens, q_home, gate_w, up_w, down_w)
    x_there = lax.all_to_all(send_x, "expert", split_axis=0, concat_axis=0, tiled=True)
    q_there = lax.all_to_all(send_q, "expert", split_axis=0, concat_axis=0, tiled=True)
    item_count = x_there.shape[1]
    hidden_there, grad_there = expert_backward(
        x_there.reshape(-1, width), q_there.reshape(-1, width), gate_w, up_w, down_w
    )
    returned = lax.all_to_all(
        grad_there.astype(jnp.bfloat16).reshape(expert_count, item_count, width),
        "expert",
        split_axis=0,
        concat_axis=0,
        tiled=True,
    )
    returned, hidden_away, q_there = (
        returned,
        hidden_there.reshape(expert_count, item_count, -1),
        q_there,
    )
    contract = (((0,), (0,)), ((), ()))
    flat_returned = returned.reshape(expert_count * capacity, width)
    grad_away = lax.dot_general(
        placing, flat_returned, contract, preferred_element_type=jnp.float32
    )
    token_grad = (grad_home + grad_away).astype(jnp.bfloat16)
    flat_hidden = hidden_away.reshape(expert_count * capacity, -1)
    flat_q = q_there.reshape(expert_count * capacity, width)
    partial = lax.dot_general(
        hidden_home, q_home, contract, preferred_element_type=jnp.float32
    ) + lax.dot_general(flat_hidden, flat_q, contract, preferred_element_type=jnp.float32)
    n_rep = lax.axis_size("replica")
    grad_down = ring_reduce_scatter(partial.reshape(n_rep, -1, partial.shape[1])).astype(
        jnp.bfloat16
    )
    return (token_grad, grad_down[None])


def solution(mesh):
    placed = (
        P(("expert", "replica"), None),
        P(("expert", "replica"), None),
        P(("expert", "replica"), None),
        P(("expert", "replica"), None),
        P(("expert", "replica")),
        P("expert", "replica", None),
        P("expert", "replica", None),
        P("expert", "replica", None),
    )
    return jax.shard_map(
        local,
        mesh=mesh,
        in_specs=placed,
        out_specs=(P(("expert", "replica"), None), P("expert", "replica", None)),
        check_vma=False,
    )
```

```python
import jax
import jax.numpy as jnp
from jax import lax
from jax.sharding import PartitionSpec as P


def against_rows(left, matrix):
    return lax.dot_general(
        left, matrix, (((1,), (1,)), ((), ())), preferred_element_type=jnp.float32
    )


def expert_backward(inputs, upstream, gate_w, up_w, down_w):
    gate_act = jnp.dot(inputs, gate_w, preferred_element_type=jnp.float32)
    up_act = jnp.dot(inputs, up_w, preferred_element_type=jnp.float32)
    sigmoid_gate = jax.nn.sigmoid(gate_act)
    swish_gate = gate_act * sigmoid_gate
    hidden = (swish_gate * up_act).astype(jnp.bfloat16)
    hidden_grad = against_rows(upstream, down_w)
    gate_grad = (
        hidden_grad * up_act * sigmoid_gate * (1.0 + gate_act * (1.0 - sigmoid_gate))
    ).astype(jnp.bfloat16)
    up_grad = (hidden_grad * swish_gate).astype(jnp.bfloat16)
    input_grad = against_rows(gate_grad, gate_w) + against_rows(up_grad, up_w)
    return (hidden, input_grad)


def ring_gather(piece, axis):
    n = lax.axis_size(axis)
    idx = lax.axis_index(axis)
    right = [(i, (i + 1) % n) for i in range(n)]
    left = [(i, (i - 1) % n) for i in range(n)]
    ahead = {0: piece}
    r = l = piece
    half = n // 2
    steps = half if n % 2 == 1 else half - 1
    for k in range(1, steps + 1):
        r = lax.ppermute(r, axis, right)
        l = lax.ppermute(l, axis, left)
        ahead[n - k] = r
        ahead[k] = l
    if n % 2 == 0 and n > 1:
        cut = piece.shape[-1] // 2
        rh = lax.ppermute(r[..., :cut], axis, right)
        lh = lax.ppermute(l[..., cut:], axis, left)
        ahead[half] = jnp.concatenate([rh, lh], axis=-1)
    stacked = jnp.stack([ahead[m] for m in range(n)])
    order = (jnp.arange(n, dtype=jnp.int32) - idx) % n
    return jnp.take(stacked, order, axis=0)


def local(tokens, cotangent, partner, combine, counts, w_gate, w_up, w_down):
    tok_rows = tokens.shape[0]
    width = tokens.shape[1]
    expert_count = lax.axis_size("expert")
    capacity = max(2, (5 * tok_rows // 4 + expert_count - 1) // expert_count)
    positions = jnp.arange(tok_rows, dtype=jnp.int32)
    valid_rows = positions < counts[0]
    weights = combine.astype(jnp.float32)
    weight_sum = weights[:, 0] + weights[:, 1]
    share_home = jnp.where(valid_rows, weights[:, 0] / weight_sum, 0.0)
    share_away = jnp.where(valid_rows, weights[:, 1] / weight_sum, 0.0)
    upstream = cotangent.astype(jnp.float32)
    q_home = (upstream * share_home[:, None]).astype(jnp.bfloat16)
    q_away = (upstream * share_away[:, None]).astype(jnp.bfloat16)
    gate_full, up_full = (
        lax.all_gather(w_gate, "replica", axis=1, tiled=True),
        lax.all_gather(w_up, "replica", axis=1, tiled=True),
    )
    down_full = ring_gather(w_down[0], "replica")
    gate_w = gate_full.reshape(gate_full.shape[1], gate_full.shape[2])
    up_w = up_full.reshape(up_full.shape[1], up_full.shape[2])
    down_w = down_full.reshape(-1, down_full.shape[2])
    target = partner[:, 0]
    onehot_rows = (target[:, None] == jnp.arange(expert_count, dtype=jnp.int32)[None, :]).astype(
        jnp.int32
    )
    rank_within = jnp.sum((jnp.cumsum(onehot_rows, axis=0) - onehot_rows) * onehot_rows, axis=1)
    destination = target * capacity + rank_within
    placing = (
        jnp.arange(expert_count * capacity, dtype=jnp.int32)[:, None] == destination[None, :]
    ).astype(jnp.bfloat16)
    send_x = (
        jnp.dot(placing, tokens, preferred_element_type=jnp.float32)
        .astype(jnp.bfloat16)
        .reshape(expert_count, capacity, width)
    )
    send_q = (
        jnp.dot(placing, q_away, preferred_element_type=jnp.float32)
        .astype(jnp.bfloat16)
        .reshape(expert_count, capacity, width)
    )
    hidden_home, grad_home = expert_backward(tokens, q_home, gate_w, up_w, down_w)
    x_there = lax.all_to_all(send_x, "expert", split_axis=0, concat_axis=0, tiled=True)
    q_there = lax.all_to_all(send_q, "expert", split_axis=0, concat_axis=0, tiled=True)
    item_count = x_there.shape[1]
    hidden_there, grad_there = expert_backward(
        x_there.reshape(-1, width), q_there.reshape(-1, width), gate_w, up_w, down_w
    )
    returned = lax.all_to_all(
        grad_there.astype(jnp.bfloat16).reshape(expert_count, item_count, width),
        "expert",
        split_axis=0,
        concat_axis=0,
        tiled=True,
    )
    returned, hidden_away, q_there = (
        returned,
        hidden_there.reshape(expert_count, item_count, -1),
        q_there,
    )
    contract = (((0,), (0,)), ((), ()))
    flat_returned = returned.reshape(expert_count * capacity, width)
    grad_away = lax.dot_general(
        placing, flat_returned, contract, preferred_element_type=jnp.float32
    )
    token_grad = (grad_home + grad_away).astype(jnp.bfloat16)
    flat_hidden = hidden_away.reshape(expert_count * capacity, -1)
    flat_q = q_there.reshape(expert_count * capacity, width)
    grad_down = lax.psum_scatter(
        (
            lax.dot_general(hidden_home, q_home, contract, preferred_element_type=jnp.float32)
            + lax.dot_general(flat_hidden, flat_q, contract, preferred_element_type=jnp.float32)
        ).astype(jnp.bfloat16),
        "replica",
        scatter_dimension=0,
        tiled=True,
    )
    return (token_grad, grad_down[None])


def solution(mesh):
    placed = (
        P(("expert", "replica"), None),
        P(("expert", "replica"), None),
        P(("expert", "replica"), None),
        P(("expert", "replica"), None),
        P(("expert", "replica")),
        P("expert", "replica", None),
        P("expert", "replica", None),
        P("expert", "replica", None),
    )
    return jax.shard_map(
        local,
        mesh=mesh,
        in_specs=placed,
        out_specs=(P(("expert", "replica"), None), P("expert", "replica", None)),
        check_vma=False,
    )
```

```python
import jax
import jax.numpy as jnp
from jax import lax
from jax.sharding import PartitionSpec as P


def against_rows(left, matrix):
    return lax.dot_general(
        left, matrix, (((1,), (1,)), ((), ())), preferred_element_type=jnp.float32
    )


def expert_backward(inputs, upstream, gate_w, up_w, down_w):
    gate_act = jnp.dot(inputs, gate_w, preferred_element_type=jnp.float32)
    up_act = jnp.dot(inputs, up_w, preferred_element_type=jnp.float32)
    sigmoid_gate = jax.nn.sigmoid(gate_act)
    swish_gate = gate_act * sigmoid_gate
    hidden = (swish_gate * up_act).astype(jnp.bfloat16)
    hidden_grad = against_rows(upstream, down_w)
    gate_grad = (
        hidden_grad * up_act * sigmoid_gate * (1.0 + gate_act * (1.0 - sigmoid_gate))
    ).astype(jnp.bfloat16)
    up_grad = (hidden_grad * swish_gate).astype(jnp.bfloat16)
    input_grad = against_rows(gate_grad, gate_w) + against_rows(up_grad, up_w)
    return (hidden, input_grad)


def ring_gather(pieces, axis):
    n = lax.axis_size(axis)
    idx = lax.axis_index(axis)
    right = [(i, (i + 1) % n) for i in range(n)]
    left = [(i, (i - 1) % n) for i in range(n)]
    ahead = [{0: p} for p in pieces]
    r, l = list(pieces), list(pieces)
    half = n // 2
    steps = half if n % 2 == 1 else half - 1
    for k in range(1, steps + 1):
        r = [lax.ppermute(p, axis, right) for p in r]
        l = [lax.ppermute(p, axis, left) for p in l]
        for a, rp, lp in zip(ahead, r, l):
            a[n - k] = rp
            a[k] = lp
    if n % 2 == 0 and n > 1:
        for a, rp, lp in zip(ahead, r, l):
            cut = rp.shape[-1] // 2
            rh = lax.ppermute(rp[..., :cut], axis, right)
            lh = lax.ppermute(lp[..., cut:], axis, left)
            a[half] = jnp.concatenate([rh, lh], axis=-1)
    order = (jnp.arange(n, dtype=jnp.int32) - idx) % n
    return [jnp.take(jnp.stack([a[m] for m in range(n)]), order, axis=0) for a in ahead]


def local(tokens, cotangent, partner, combine, counts, w_gate, w_up, w_down):
    tok_rows = tokens.shape[0]
    width = tokens.shape[1]
    expert_count = lax.axis_size("expert")
    capacity = max(2, (5 * tok_rows // 4 + expert_count - 1) // expert_count)
    positions = jnp.arange(tok_rows, dtype=jnp.int32)
    valid_rows = positions < counts[0]
    weights = combine.astype(jnp.float32)
    weight_sum = weights[:, 0] + weights[:, 1]
    share_home = jnp.where(valid_rows, weights[:, 0] / weight_sum, 0.0)
    share_away = jnp.where(valid_rows, weights[:, 1] / weight_sum, 0.0)
    upstream = cotangent.astype(jnp.float32)
    q_home = (upstream * share_home[:, None]).astype(jnp.bfloat16)
    q_away = (upstream * share_away[:, None]).astype(jnp.bfloat16)
    split = w_up.shape[2] // 2
    gate_full, up_first = (
        lax.all_gather(w_gate, "replica", axis=1, tiled=True),
        lax.all_gather(w_up[..., :split], "replica", axis=1, tiled=True),
    )
    down_full, up_second = ring_gather([w_down[0], w_up[0, :, split:]], "replica")
    gate_w = gate_full.reshape(gate_full.shape[1], gate_full.shape[2])
    up_w = jnp.concatenate(
        [up_first.reshape(up_first.shape[1], split), up_second.reshape(-1, w_up.shape[2] - split)],
        axis=1,
    )
    down_w = down_full.reshape(-1, down_full.shape[2])
    target = partner[:, 0]
    onehot_rows = (target[:, None] == jnp.arange(expert_count, dtype=jnp.int32)[None, :]).astype(
        jnp.int32
    )
    rank_within = jnp.sum((jnp.cumsum(onehot_rows, axis=0) - onehot_rows) * onehot_rows, axis=1)
    destination = target * capacity + rank_within
    placing = (
        jnp.arange(expert_count * capacity, dtype=jnp.int32)[:, None] == destination[None, :]
    ).astype(jnp.bfloat16)
    send_x = (
        jnp.dot(placing, tokens, preferred_element_type=jnp.float32)
        .astype(jnp.bfloat16)
        .reshape(expert_count, capacity, width)
    )
    send_q = (
        jnp.dot(placing, q_away, preferred_element_type=jnp.float32)
        .astype(jnp.bfloat16)
        .reshape(expert_count, capacity, width)
    )
    hidden_home, grad_home = expert_backward(tokens, q_home, gate_w, up_w, down_w)
    x_there = lax.all_to_all(send_x, "expert", split_axis=0, concat_axis=0, tiled=True)
    q_there = lax.all_to_all(send_q, "expert", split_axis=0, concat_axis=0, tiled=True)
    item_count = x_there.shape[1]
    hidden_there, grad_there = expert_backward(
        x_there.reshape(-1, width), q_there.reshape(-1, width), gate_w, up_w, down_w
    )
    returned = lax.all_to_all(
        grad_there.astype(jnp.bfloat16).reshape(expert_count, item_count, width),
        "expert",
        split_axis=0,
        concat_axis=0,
        tiled=True,
    )
    returned, hidden_away, q_there = (
        returned,
        hidden_there.reshape(expert_count, item_count, -1),
        q_there,
    )
    contract = (((0,), (0,)), ((), ()))
    flat_returned = returned.reshape(expert_count * capacity, width)
    grad_away = lax.dot_general(
        placing, flat_returned, contract, preferred_element_type=jnp.float32
    )
    token_grad = (grad_home + grad_away).astype(jnp.bfloat16)
    flat_hidden = hidden_away.reshape(expert_count * capacity, -1)
    flat_q = q_there.reshape(expert_count * capacity, width)
    grad_down = lax.psum_scatter(
        (
            lax.dot_general(hidden_home, q_home, contract, preferred_element_type=jnp.float32)
            + lax.dot_general(flat_hidden, flat_q, contract, preferred_element_type=jnp.float32)
        ).astype(jnp.bfloat16),
        "replica",
        scatter_dimension=0,
        tiled=True,
    )
    return (token_grad, grad_down[None])


def solution(mesh):
    placed = (
        P(("expert", "replica"), None),
        P(("expert", "replica"), None),
        P(("expert", "replica"), None),
        P(("expert", "replica"), None),
        P(("expert", "replica")),
        P("expert", "replica", None),
        P("expert", "replica", None),
        P("expert", "replica", None),
    )
    return jax.shard_map(
        local,
        mesh=mesh,
        in_specs=placed,
        out_specs=(P(("expert", "replica"), None), P("expert", "replica", None)),
        check_vma=False,
    )
```

```python
import jax
import jax.numpy as jnp
from jax import lax
from jax.sharding import PartitionSpec as P


def against_rows(left, matrix):
    return lax.dot_general(
        left, matrix, (((1,), (1,)), ((), ())), preferred_element_type=jnp.float32
    )


def expert_backward(inputs, upstream, gate_w, up_w, down_w):
    gate_act = jnp.dot(inputs, gate_w, preferred_element_type=jnp.float32)
    up_act = jnp.dot(inputs, up_w, preferred_element_type=jnp.float32)
    sigmoid_gate = jax.nn.sigmoid(gate_act)
    swish_gate = gate_act * sigmoid_gate
    hidden = (swish_gate * up_act).astype(jnp.bfloat16)
    hidden_grad = against_rows(upstream, down_w)
    gate_grad = (
        hidden_grad * up_act * sigmoid_gate * (1.0 + gate_act * (1.0 - sigmoid_gate))
    ).astype(jnp.bfloat16)
    up_grad = (hidden_grad * swish_gate).astype(jnp.bfloat16)
    input_grad = against_rows(gate_grad, gate_w) + against_rows(up_grad, up_w)
    return (hidden, input_grad)


def local(tokens, cotangent, partner, combine, counts, w_gate, w_up, w_down):
    tok_rows = tokens.shape[0]
    width = tokens.shape[1]
    expert_count = lax.axis_size("expert")
    capacity = max(2, (5 * tok_rows // 4 + expert_count - 1) // expert_count)
    positions = jnp.arange(tok_rows, dtype=jnp.int32)
    valid_rows = positions < counts[0]
    weights = combine.astype(jnp.float32)
    weight_sum = weights[:, 0] + weights[:, 1]
    share_home = jnp.where(valid_rows, weights[:, 0] / weight_sum, 0.0)
    share_away = jnp.where(valid_rows, weights[:, 1] / weight_sum, 0.0)
    upstream = cotangent.astype(jnp.float32)
    q_home = (upstream * share_home[:, None]).astype(jnp.bfloat16)
    q_away = (upstream * share_away[:, None]).astype(jnp.bfloat16)
    shard_rows, hidden_units = w_gate.shape[1], w_gate.shape[2]
    stacked = jnp.stack([w_gate[0], w_up[0], w_down[0].reshape(shard_rows, hidden_units)])
    full = lax.all_gather(stacked, "replica", axis=0, tiled=False)
    gate_w = full[:, 0].reshape(-1, hidden_units)
    up_w = full[:, 1].reshape(-1, hidden_units)
    down_w = full[:, 2].reshape(-1, w_down.shape[1], w_down.shape[2]).reshape(-1, w_down.shape[2])
    target = partner[:, 0]
    onehot_rows = (target[:, None] == jnp.arange(expert_count, dtype=jnp.int32)[None, :]).astype(
        jnp.int32
    )
    rank_within = jnp.sum((jnp.cumsum(onehot_rows, axis=0) - onehot_rows) * onehot_rows, axis=1)
    destination = target * capacity + rank_within
    placing = (
        jnp.arange(expert_count * capacity, dtype=jnp.int32)[:, None] == destination[None, :]
    ).astype(jnp.bfloat16)
    send_x = (
        jnp.dot(placing, tokens, preferred_element_type=jnp.float32)
        .astype(jnp.bfloat16)
        .reshape(expert_count, capacity, width)
    )
    send_q = (
        jnp.dot(placing, q_away, preferred_element_type=jnp.float32)
        .astype(jnp.bfloat16)
        .reshape(expert_count, capacity, width)
    )
    hidden_home, grad_home = expert_backward(tokens, q_home, gate_w, up_w, down_w)
    x_there = lax.all_to_all(send_x, "expert", split_axis=0, concat_axis=0, tiled=True)
    q_there = lax.all_to_all(send_q, "expert", split_axis=0, concat_axis=0, tiled=True)
    item_count = x_there.shape[1]
    hidden_there, grad_there = expert_backward(
        x_there.reshape(-1, width), q_there.reshape(-1, width), gate_w, up_w, down_w
    )
    returned = lax.all_to_all(
        grad_there.astype(jnp.bfloat16).reshape(expert_count, item_count, width),
        "expert",
        split_axis=0,
        concat_axis=0,
        tiled=True,
    )
    returned, hidden_away, q_there = (
        returned,
        hidden_there.reshape(expert_count, item_count, -1),
        q_there,
    )
    contract = (((0,), (0,)), ((), ()))
    flat_returned = returned.reshape(expert_count * capacity, width)
    grad_away = lax.dot_general(
        placing, flat_returned, contract, preferred_element_type=jnp.float32
    )
    token_grad = (grad_home + grad_away).astype(jnp.bfloat16)
    flat_hidden = hidden_away.reshape(expert_count * capacity, -1)
    flat_q = q_there.reshape(expert_count * capacity, width)
    grad_down = lax.psum_scatter(
        (
            lax.dot_general(hidden_home, q_home, contract, preferred_element_type=jnp.float32)
            + lax.dot_general(flat_hidden, flat_q, contract, preferred_element_type=jnp.float32)
        ).astype(jnp.bfloat16),
        "replica",
        scatter_dimension=0,
        tiled=True,
    )
    return (token_grad, grad_down[None])


def solution(mesh):
    placed = (
        P(("expert", "replica"), None),
        P(("expert", "replica"), None),
        P(("expert", "replica"), None),
        P(("expert", "replica"), None),
        P(("expert", "replica")),
        P("expert", "replica", None),
        P("expert", "replica", None),
        P("expert", "replica", None),
    )
    return jax.shard_map(
        local,
        mesh=mesh,
        in_specs=placed,
        out_specs=(P(("expert", "replica"), None), P("expert", "replica", None)),
        check_vma=False,
    )
```

```python
import jax
import jax.numpy as jnp
from jax import lax
from jax.sharding import PartitionSpec as P


def against_rows(left, matrix):
    return lax.dot_general(
        left, matrix, (((1,), (1,)), ((), ())), preferred_element_type=jnp.float32
    )


def expert_backward(inputs, upstream, gate_w, up_w, down_w):
    gate_act = jnp.dot(inputs, gate_w, preferred_element_type=jnp.float32)
    up_act = jnp.dot(inputs, up_w, preferred_element_type=jnp.float32)
    sigmoid_gate = jax.nn.sigmoid(gate_act)
    swish_gate = gate_act * sigmoid_gate
    hidden = (swish_gate * up_act).astype(jnp.bfloat16)
    hidden_grad = against_rows(upstream, down_w)
    gate_grad = (
        hidden_grad * up_act * sigmoid_gate * (1.0 + gate_act * (1.0 - sigmoid_gate))
    ).astype(jnp.bfloat16)
    up_grad = (hidden_grad * swish_gate).astype(jnp.bfloat16)
    input_grad = against_rows(gate_grad, gate_w) + against_rows(up_grad, up_w)
    return (hidden, input_grad)


def ring_gather(piece, axis):
    n = lax.axis_size(axis)
    idx = lax.axis_index(axis)
    right = [(i, (i + 1) % n) for i in range(n)]
    left = [(i, (i - 1) % n) for i in range(n)]
    ahead = {0: piece}
    r = l = piece
    half = n // 2
    steps = half if n % 2 == 1 else half - 1
    for k in range(1, steps + 1):
        r = lax.ppermute(r, axis, right)
        l = lax.ppermute(l, axis, left)
        ahead[n - k] = r
        ahead[k] = l
    if n % 2 == 0 and n > 1:
        cut = piece.shape[-1] // 2
        rh = lax.ppermute(r[..., :cut], axis, right)
        lh = lax.ppermute(l[..., cut:], axis, left)
        ahead[half] = jnp.concatenate([rh, lh], axis=-1)
    stacked = jnp.stack([ahead[m] for m in range(n)])
    order = (jnp.arange(n, dtype=jnp.int32) - idx) % n
    return jnp.take(stacked, order, axis=0)


def local(tokens, cotangent, partner, combine, counts, w_gate, w_up, w_down):
    tok_rows = tokens.shape[0]
    width = tokens.shape[1]
    expert_count = lax.axis_size("expert")
    capacity = max(2, (5 * tok_rows // 4 + expert_count - 1) // expert_count)
    positions = jnp.arange(tok_rows, dtype=jnp.int32)
    valid_rows = positions < counts[0]
    weights = combine.astype(jnp.float32)
    weight_sum = weights[:, 0] + weights[:, 1]
    share_home = jnp.where(valid_rows, weights[:, 0] / weight_sum, 0.0)
    share_away = jnp.where(valid_rows, weights[:, 1] / weight_sum, 0.0)
    upstream = cotangent.astype(jnp.float32)
    q_home = (upstream * share_home[:, None]).astype(jnp.bfloat16)
    q_away = (upstream * share_away[:, None]).astype(jnp.bfloat16)
    pair = lax.all_gather(jnp.stack([w_gate[0], w_up[0]]), "replica", axis=0, tiled=False)
    down_full = ring_gather(w_down[0], "replica")
    gate_w = pair[:, 0].reshape(-1, w_gate.shape[2])
    up_w = pair[:, 1].reshape(-1, w_up.shape[2])
    down_w = down_full.reshape(-1, down_full.shape[2])
    target = partner[:, 0]
    onehot_rows = (target[:, None] == jnp.arange(expert_count, dtype=jnp.int32)[None, :]).astype(
        jnp.int32
    )
    rank_within = jnp.sum((jnp.cumsum(onehot_rows, axis=0) - onehot_rows) * onehot_rows, axis=1)
    destination = target * capacity + rank_within
    placing = (
        jnp.arange(expert_count * capacity, dtype=jnp.int32)[:, None] == destination[None, :]
    ).astype(jnp.bfloat16)
    send_x = (
        jnp.dot(placing, tokens, preferred_element_type=jnp.float32)
        .astype(jnp.bfloat16)
        .reshape(expert_count, capacity, width)
    )
    send_q = (
        jnp.dot(placing, q_away, preferred_element_type=jnp.float32)
        .astype(jnp.bfloat16)
        .reshape(expert_count, capacity, width)
    )
    hidden_home, grad_home = expert_backward(tokens, q_home, gate_w, up_w, down_w)
    x_there = lax.all_to_all(send_x, "expert", split_axis=0, concat_axis=0, tiled=True)
    q_there = lax.all_to_all(send_q, "expert", split_axis=0, concat_axis=0, tiled=True)
    item_count = x_there.shape[1]
    hidden_there, grad_there = expert_backward(
        x_there.reshape(-1, width), q_there.reshape(-1, width), gate_w, up_w, down_w
    )
    returned = lax.all_to_all(
        grad_there.astype(jnp.bfloat16).reshape(expert_count, item_count, width),
        "expert",
        split_axis=0,
        concat_axis=0,
        tiled=True,
    )
    returned, hidden_away, q_there = (
        returned,
        hidden_there.reshape(expert_count, item_count, -1),
        q_there,
    )
    contract = (((0,), (0,)), ((), ()))
    flat_returned = returned.reshape(expert_count * capacity, width)
    grad_away = lax.dot_general(
        placing, flat_returned, contract, preferred_element_type=jnp.float32
    )
    token_grad = (grad_home + grad_away).astype(jnp.bfloat16)
    flat_hidden = hidden_away.reshape(expert_count * capacity, -1)
    flat_q = q_there.reshape(expert_count * capacity, width)
    grad_down = lax.psum_scatter(
        (
            lax.dot_general(hidden_home, q_home, contract, preferred_element_type=jnp.float32)
            + lax.dot_general(flat_hidden, flat_q, contract, preferred_element_type=jnp.float32)
        ).astype(jnp.bfloat16),
        "replica",
        scatter_dimension=0,
        tiled=True,
    )
    return (token_grad, grad_down[None])


def solution(mesh):
    placed = (
        P(("expert", "replica"), None),
        P(("expert", "replica"), None),
        P(("expert", "replica"), None),
        P(("expert", "replica"), None),
        P(("expert", "replica")),
        P("expert", "replica", None),
        P("expert", "replica", None),
        P("expert", "replica", None),
    )
    return jax.shard_map(
        local,
        mesh=mesh,
        in_specs=placed,
        out_specs=(P(("expert", "replica"), None), P("expert", "replica", None)),
        check_vma=False,
    )
```

```python
import jax
import jax.numpy as jnp
from jax import lax
from jax.sharding import PartitionSpec as P


def against_rows(left, matrix):
    return lax.dot_general(
        left, matrix, (((1,), (1,)), ((), ())), preferred_element_type=jnp.float32
    )


def expert_backward(inputs, upstream, gate_w, up_w, down_w):
    gate_act = jnp.dot(inputs, gate_w, preferred_element_type=jnp.float32)
    up_act = jnp.dot(inputs, up_w, preferred_element_type=jnp.float32)
    sigmoid_gate = jax.nn.sigmoid(gate_act)
    swish_gate = gate_act * sigmoid_gate
    hidden = (swish_gate * up_act).astype(jnp.bfloat16)
    hidden_grad = against_rows(upstream, down_w)
    gate_grad = (
        hidden_grad * up_act * sigmoid_gate * (1.0 + gate_act * (1.0 - sigmoid_gate))
    ).astype(jnp.bfloat16)
    up_grad = (hidden_grad * swish_gate).astype(jnp.bfloat16)
    input_grad = against_rows(gate_grad, gate_w) + against_rows(up_grad, up_w)
    return (hidden, input_grad)


def ring_gather(piece, axis):
    n = lax.axis_size(axis[0]) * lax.axis_size(axis[1])
    idx = lax.axis_index(axis[0]) * lax.axis_size(axis[1]) + lax.axis_index(axis[1])
    right = [(i, (i + 1) % n) for i in range(n)]
    left = [(i, (i - 1) % n) for i in range(n)]
    ahead = {0: piece}
    r = l = piece
    half = n // 2
    steps = half if n % 2 == 1 else half - 1
    for k in range(1, steps + 1):
        r = lax.ppermute(r, axis, right)
        l = lax.ppermute(l, axis, left)
        ahead[n - k] = r
        ahead[k] = l
    if n % 2 == 0 and n > 1:
        cut = piece.shape[-1] // 2
        rh = lax.ppermute(r[..., :cut], axis, right)
        lh = lax.ppermute(l[..., cut:], axis, left)
        ahead[half] = jnp.concatenate([rh, lh], axis=-1)
    stacked = jnp.stack([ahead[m] for m in range(n)])
    order = (jnp.arange(n, dtype=jnp.int32) - idx) % n
    return jnp.take(stacked, order, axis=0)


REPLICA = ("zhi", "zlo")


def local(tokens, cotangent, partner, combine, counts, w_gate, w_up, w_down):
    tok_rows = tokens.shape[0]
    width = tokens.shape[1]
    expert_count = lax.axis_size("expert")
    capacity = max(2, (5 * tok_rows // 4 + expert_count - 1) // expert_count)
    positions = jnp.arange(tok_rows, dtype=jnp.int32)
    valid_rows = positions < counts[0]
    weights = combine.astype(jnp.float32)
    weight_sum = weights[:, 0] + weights[:, 1]
    share_home = jnp.where(valid_rows, weights[:, 0] / weight_sum, 0.0)
    share_away = jnp.where(valid_rows, weights[:, 1] / weight_sum, 0.0)
    upstream = cotangent.astype(jnp.float32)
    q_home = (upstream * share_home[:, None]).astype(jnp.bfloat16)
    q_away = (upstream * share_away[:, None]).astype(jnp.bfloat16)
    pair = lax.all_gather(jnp.stack([w_gate[0], w_up[0]]), REPLICA, axis=0, tiled=False)
    down_full = ring_gather(w_down[0], REPLICA)
    gate_w = pair[:, 0].reshape(-1, w_gate.shape[2])
    up_w = pair[:, 1].reshape(-1, w_up.shape[2])
    down_w = down_full.reshape(-1, down_full.shape[2])
    target = partner[:, 0]
    onehot_rows = (target[:, None] == jnp.arange(expert_count, dtype=jnp.int32)[None, :]).astype(
        jnp.int32
    )
    rank_within = jnp.sum((jnp.cumsum(onehot_rows, axis=0) - onehot_rows) * onehot_rows, axis=1)
    destination = target * capacity + rank_within
    placing = (
        jnp.arange(expert_count * capacity, dtype=jnp.int32)[:, None] == destination[None, :]
    ).astype(jnp.bfloat16)
    send_x = (
        jnp.dot(placing, tokens, preferred_element_type=jnp.float32)
        .astype(jnp.bfloat16)
        .reshape(expert_count, capacity, width)
    )
    send_q = (
        jnp.dot(placing, q_away, preferred_element_type=jnp.float32)
        .astype(jnp.bfloat16)
        .reshape(expert_count, capacity, width)
    )
    hidden_home, grad_home = expert_backward(tokens, q_home, gate_w, up_w, down_w)
    x_there = lax.all_to_all(send_x, "expert", split_axis=0, concat_axis=0, tiled=True)
    q_there = lax.all_to_all(send_q, "expert", split_axis=0, concat_axis=0, tiled=True)
    item_count = x_there.shape[1]
    hidden_there, grad_there = expert_backward(
        x_there.reshape(-1, width), q_there.reshape(-1, width), gate_w, up_w, down_w
    )
    returned = lax.all_to_all(
        grad_there.astype(jnp.bfloat16).reshape(expert_count, item_count, width),
        "expert",
        split_axis=0,
        concat_axis=0,
        tiled=True,
    )
    returned, hidden_away, q_there = (
        returned,
        hidden_there.reshape(expert_count, item_count, -1),
        q_there,
    )
    contract = (((0,), (0,)), ((), ()))
    flat_returned = returned.reshape(expert_count * capacity, width)
    grad_away = lax.dot_general(
        placing, flat_returned, contract, preferred_element_type=jnp.float32
    )
    token_grad = (grad_home + grad_away).astype(jnp.bfloat16)
    flat_hidden = hidden_away.reshape(expert_count * capacity, -1)
    flat_q = q_there.reshape(expert_count * capacity, width)
    n_hi, n_lo = lax.axis_size(REPLICA[0]), lax.axis_size(REPLICA[1])

    def lo_major(h):
        rows = h.shape[0]
        return h.reshape(rows, n_hi, n_lo, -1).transpose(0, 2, 1, 3).reshape(rows, -1)

    partial = (
        lax.dot_general(lo_major(hidden_home), q_home, contract, preferred_element_type=jnp.float32)
        + lax.dot_general(lo_major(flat_hidden), flat_q, contract, preferred_element_type=jnp.float32)
    ).astype(jnp.bfloat16)
    grad_down = lax.psum_scatter(partial, REPLICA[1], scatter_dimension=0, tiled=True)
    grad_down = lax.psum_scatter(grad_down, REPLICA[0], scatter_dimension=0, tiled=True)
    return (token_grad, grad_down[None])


def solution(mesh):
    n_rep = mesh.shape["replica"]
    n_lo = 4 if n_rep % 4 == 0 else 1
    grid = jax.sharding.Mesh(
        mesh.devices.reshape(mesh.shape["expert"], n_rep // n_lo, n_lo), ("expert",) + REPLICA
    )
    rows = P(("expert",) + REPLICA, None)
    weight = P("expert", REPLICA, None)
    placed = (rows, rows, rows, rows, P(("expert",) + REPLICA), weight, weight, weight)
    return jax.shard_map(
        local,
        mesh=grid,
        in_specs=placed,
        out_specs=(rows, weight),
        check_vma=False,
    )
```

```python
import jax
import jax.numpy as jnp
from jax import lax
from jax.sharding import PartitionSpec as P


def against_rows(left, matrix):
    return lax.dot_general(
        left, matrix, (((1,), (1,)), ((), ())), preferred_element_type=jnp.float32
    )


def expert_backward(inputs, upstream, gate_w, up_w, down_w):
    gate_act = jnp.dot(inputs, gate_w, preferred_element_type=jnp.float32)
    up_act = jnp.dot(inputs, up_w, preferred_element_type=jnp.float32)
    sigmoid_gate = jax.nn.sigmoid(gate_act)
    swish_gate = gate_act * sigmoid_gate
    hidden = (swish_gate * up_act).astype(jnp.bfloat16)
    hidden_grad = against_rows(upstream, down_w)
    gate_grad = (
        hidden_grad * up_act * sigmoid_gate * (1.0 + gate_act * (1.0 - sigmoid_gate))
    ).astype(jnp.bfloat16)
    up_grad = (hidden_grad * swish_gate).astype(jnp.bfloat16)
    input_grad = against_rows(gate_grad, gate_w) + against_rows(up_grad, up_w)
    return (hidden, input_grad)


def ring_gather(piece, axis):
    n = lax.axis_size(axis)
    idx = lax.axis_index(axis)
    right = [(i, (i + 1) % n) for i in range(n)]
    left = [(i, (i - 1) % n) for i in range(n)]
    ahead = {0: piece}
    r = l = piece
    half = n // 2
    steps = half if n % 2 == 1 else half - 1
    for k in range(1, steps + 1):
        r = lax.ppermute(r, axis, right)
        l = lax.ppermute(l, axis, left)
        ahead[n - k] = r
        ahead[k] = l
    if n % 2 == 0 and n > 1:
        cut = piece.shape[-1] // 2
        rh = lax.ppermute(r[..., :cut], axis, right)
        lh = lax.ppermute(l[..., cut:], axis, left)
        ahead[half] = jnp.concatenate([rh, lh], axis=-1)
    stacked = jnp.stack([ahead[m] for m in range(n)])
    order = (jnp.arange(n, dtype=jnp.int32) - idx) % n
    return jnp.take(stacked, order, axis=0)


def local(tokens, cotangent, partner, combine, counts, w_gate, w_up, w_down):
    tok_rows = tokens.shape[0]
    width = tokens.shape[1]
    expert_count = lax.axis_size("expert")
    capacity = max(2, (5 * tok_rows // 4 + expert_count - 1) // expert_count)
    positions = jnp.arange(tok_rows, dtype=jnp.int32)
    valid_rows = positions < counts[0]
    weights = combine.astype(jnp.float32)
    weight_sum = weights[:, 0] + weights[:, 1]
    share_home = jnp.where(valid_rows, weights[:, 0] / weight_sum, 0.0)
    share_away = jnp.where(valid_rows, weights[:, 1] / weight_sum, 0.0)
    upstream = cotangent.astype(jnp.float32)
    q_home = (upstream * share_home[:, None]).astype(jnp.bfloat16)
    q_away = (upstream * share_away[:, None]).astype(jnp.bfloat16)
    pair = lax.all_gather(jnp.stack([w_gate[0], w_up[0]]), "replica", axis=0, tiled=False)
    down_full = ring_gather(w_down[0], "replica")
    gate_w = pair[:, 0].reshape(-1, w_gate.shape[2])
    up_w = pair[:, 1].reshape(-1, w_up.shape[2])
    down_w = down_full.reshape(-1, down_full.shape[2])
    target = partner[:, 0]
    onehot_rows = (target[:, None] == jnp.arange(expert_count, dtype=jnp.int32)[None, :]).astype(
        jnp.int32
    )
    rank_within = jnp.sum((jnp.cumsum(onehot_rows, axis=0) - onehot_rows) * onehot_rows, axis=1)
    destination = target * capacity + rank_within
    placing = (
        jnp.arange(expert_count * capacity, dtype=jnp.int32)[:, None] == destination[None, :]
    ).astype(jnp.bfloat16)
    send_x = (
        jnp.dot(placing, tokens, preferred_element_type=jnp.float32)
        .astype(jnp.bfloat16)
        .reshape(expert_count, capacity, width)
    )
    send_q = (
        jnp.dot(placing, q_away, preferred_element_type=jnp.float32)
        .astype(jnp.bfloat16)
        .reshape(expert_count, capacity, width)
    )
    x_there = lax.all_to_all(send_x, "expert", split_axis=0, concat_axis=0, tiled=True)
    q_there = lax.all_to_all(send_q, "expert", split_axis=0, concat_axis=0, tiled=True)
    item_count = x_there.shape[1]
    rows_in = jnp.concatenate([tokens, x_there.reshape(-1, width)], axis=0)
    q_in = jnp.concatenate([q_home, q_there.reshape(-1, width)], axis=0)
    hidden_all, grad_all = expert_backward(rows_in, q_in, gate_w, up_w, down_w)
    grad_home = grad_all[:tok_rows]
    grad_there = grad_all[tok_rows:]
    returned = lax.all_to_all(
        grad_there.astype(jnp.bfloat16).reshape(expert_count, item_count, width),
        "expert",
        split_axis=0,
        concat_axis=0,
        tiled=True,
    )
    contract = (((0,), (0,)), ((), ()))
    flat_returned = returned.reshape(expert_count * capacity, width)
    grad_away = lax.dot_general(
        placing, flat_returned, contract, preferred_element_type=jnp.float32
    )
    token_grad = (grad_home + grad_away).astype(jnp.bfloat16)
    grad_down = lax.psum_scatter(
        lax.dot_general(hidden_all, q_in, contract, preferred_element_type=jnp.float32).astype(
            jnp.bfloat16
        ),
        "replica",
        scatter_dimension=0,
        tiled=True,
    )
    return (token_grad, grad_down[None])


def solution(mesh):
    placed = (
        P(("expert", "replica"), None),
        P(("expert", "replica"), None),
        P(("expert", "replica"), None),
        P(("expert", "replica"), None),
        P(("expert", "replica")),
        P("expert", "replica", None),
        P("expert", "replica", None),
        P("expert", "replica", None),
    )
    return jax.shard_map(
        local,
        mesh=mesh,
        in_specs=placed,
        out_specs=(P(("expert", "replica"), None), P("expert", "replica", None)),
        check_vma=False,
    )
```

```python
import jax
import jax.numpy as jnp
from jax import lax
from jax.sharding import PartitionSpec as P


def against_rows(left, matrix):
    return lax.dot_general(
        left, matrix, (((1,), (1,)), ((), ())), preferred_element_type=jnp.float32
    )


def expert_backward(inputs, upstream, gate_w, up_w, down_w):
    gate_act = jnp.dot(inputs, gate_w, preferred_element_type=jnp.float32)
    up_act = jnp.dot(inputs, up_w, preferred_element_type=jnp.float32)
    sigmoid_gate = jax.nn.sigmoid(gate_act)
    swish_gate = gate_act * sigmoid_gate
    hidden = (swish_gate * up_act).astype(jnp.bfloat16)
    hidden_grad = against_rows(upstream, down_w)
    gate_grad = (
        hidden_grad * up_act * sigmoid_gate * (1.0 + gate_act * (1.0 - sigmoid_gate))
    ).astype(jnp.bfloat16)
    up_grad = (hidden_grad * swish_gate).astype(jnp.bfloat16)
    input_grad = against_rows(gate_grad, gate_w) + against_rows(up_grad, up_w)
    return (hidden, input_grad)


def ring_gather(piece, axis):
    n = lax.axis_size(axis)
    idx = lax.axis_index(axis)
    right = [(i, (i + 1) % n) for i in range(n)]
    left = [(i, (i - 1) % n) for i in range(n)]
    ahead = {0: piece}
    r = l = piece
    half = n // 2
    steps = half if n % 2 == 1 else half - 1
    for k in range(1, steps + 1):
        r = lax.ppermute(r, axis, right)
        l = lax.ppermute(l, axis, left)
        ahead[n - k] = r
        ahead[k] = l
    if n % 2 == 0 and n > 1:
        cut = piece.shape[-1] // 2
        rh = lax.ppermute(r[..., :cut], axis, right)
        lh = lax.ppermute(l[..., cut:], axis, left)
        ahead[half] = jnp.concatenate([rh, lh], axis=-1)
    stacked = jnp.stack([ahead[m] for m in range(n)])
    order = (jnp.arange(n, dtype=jnp.int32) - idx) % n
    return jnp.take(stacked, order, axis=0)


def local(tokens, cotangent, partner, combine, counts, w_gate, w_up, w_down):
    tok_rows = tokens.shape[0]
    width = tokens.shape[1]
    expert_count = lax.axis_size("expert")
    capacity = max(2, (5 * tok_rows // 4 + expert_count - 1) // expert_count)
    positions = jnp.arange(tok_rows, dtype=jnp.int32)
    valid_rows = positions < counts[0]
    weights = combine.astype(jnp.float32)
    weight_sum = weights[:, 0] + weights[:, 1]
    share_home = jnp.where(valid_rows, weights[:, 0] / weight_sum, 0.0)
    share_away = jnp.where(valid_rows, weights[:, 1] / weight_sum, 0.0)
    upstream = cotangent.astype(jnp.float32)
    q_home = (upstream * share_home[:, None]).astype(jnp.bfloat16)
    q_away = (upstream * share_away[:, None]).astype(jnp.bfloat16)
    shard_rows, hidden_units = w_gate.shape[1], w_gate.shape[2]
    down_rows, width_down = w_down.shape[1], w_down.shape[2]
    cut = width_down // 2
    packed = jnp.concatenate(
        [w_gate[0], w_up[0], w_down[0, :, :cut].reshape(-1, hidden_units)], axis=0
    )
    full = lax.all_gather(packed, "replica", axis=0, tiled=False)
    down_second = ring_gather(w_down[0, :, cut:], "replica")
    gate_w = full[:, :shard_rows].reshape(-1, hidden_units)
    up_w = full[:, shard_rows : 2 * shard_rows].reshape(-1, hidden_units)
    down_first = full[:, 2 * shard_rows :].reshape(-1, down_rows, cut)
    down_w = jnp.concatenate([down_first, down_second], axis=2).reshape(-1, width_down)
    target = partner[:, 0]
    onehot_rows = (target[:, None] == jnp.arange(expert_count, dtype=jnp.int32)[None, :]).astype(
        jnp.int32
    )
    rank_within = jnp.sum((jnp.cumsum(onehot_rows, axis=0) - onehot_rows) * onehot_rows, axis=1)
    destination = target * capacity + rank_within
    placing = (
        jnp.arange(expert_count * capacity, dtype=jnp.int32)[:, None] == destination[None, :]
    ).astype(jnp.bfloat16)
    send_x = (
        jnp.dot(placing, tokens, preferred_element_type=jnp.float32)
        .astype(jnp.bfloat16)
        .reshape(expert_count, capacity, width)
    )
    send_q = (
        jnp.dot(placing, q_away, preferred_element_type=jnp.float32)
        .astype(jnp.bfloat16)
        .reshape(expert_count, capacity, width)
    )
    hidden_home, grad_home = expert_backward(tokens, q_home, gate_w, up_w, down_w)
    x_there = lax.all_to_all(send_x, "expert", split_axis=0, concat_axis=0, tiled=True)
    q_there = lax.all_to_all(send_q, "expert", split_axis=0, concat_axis=0, tiled=True)
    item_count = x_there.shape[1]
    hidden_there, grad_there = expert_backward(
        x_there.reshape(-1, width), q_there.reshape(-1, width), gate_w, up_w, down_w
    )
    returned = lax.all_to_all(
        grad_there.astype(jnp.bfloat16).reshape(expert_count, item_count, width),
        "expert",
        split_axis=0,
        concat_axis=0,
        tiled=True,
    )
    returned, hidden_away, q_there = (
        returned,
        hidden_there.reshape(expert_count, item_count, -1),
        q_there,
    )
    contract = (((0,), (0,)), ((), ()))
    flat_returned = returned.reshape(expert_count * capacity, width)
    grad_away = lax.dot_general(
        placing, flat_returned, contract, preferred_element_type=jnp.float32
    )
    token_grad = (grad_home + grad_away).astype(jnp.bfloat16)
    flat_hidden = hidden_away.reshape(expert_count * capacity, -1)
    flat_q = q_there.reshape(expert_count * capacity, width)
    grad_down = lax.psum_scatter(
        (
            lax.dot_general(hidden_home, q_home, contract, preferred_element_type=jnp.float32)
            + lax.dot_general(flat_hidden, flat_q, contract, preferred_element_type=jnp.float32)
        ).astype(jnp.bfloat16),
        "replica",
        scatter_dimension=0,
        tiled=True,
    )
    return (token_grad, grad_down[None])


def solution(mesh):
    placed = (
        P(("expert", "replica"), None),
        P(("expert", "replica"), None),
        P(("expert", "replica"), None),
        P(("expert", "replica"), None),
        P(("expert", "replica")),
        P("expert", "replica", None),
        P("expert", "replica", None),
        P("expert", "replica", None),
    )
    return jax.shard_map(
        local,
        mesh=mesh,
        in_specs=placed,
        out_specs=(P(("expert", "replica"), None), P("expert", "replica", None)),
        check_vma=False,
    )
```

```python
import jax
import jax.numpy as jnp
from jax import lax
from jax.sharding import PartitionSpec as P


def against_rows(left, matrix):
    return lax.dot_general(
        left, matrix, (((1,), (1,)), ((), ())), preferred_element_type=jnp.float32
    )


def expert_backward(inputs, upstream, gate_w, up_w, down_w):
    gate_act = jnp.dot(inputs, gate_w, preferred_element_type=jnp.float32)
    up_act = jnp.dot(inputs, up_w, preferred_element_type=jnp.float32)
    sigmoid_gate = jax.nn.sigmoid(gate_act)
    swish_gate = gate_act * sigmoid_gate
    hidden = (swish_gate * up_act).astype(jnp.bfloat16)
    hidden_grad = against_rows(upstream, down_w)
    gate_grad = (
        hidden_grad * up_act * sigmoid_gate * (1.0 + gate_act * (1.0 - sigmoid_gate))
    ).astype(jnp.bfloat16)
    up_grad = (hidden_grad * swish_gate).astype(jnp.bfloat16)
    input_grad = against_rows(gate_grad, gate_w) + against_rows(up_grad, up_w)
    return (hidden, input_grad)


def ring_gather(piece, axis):
    n = lax.axis_size(axis)
    idx = lax.axis_index(axis)
    right = [(i, (i + 1) % n) for i in range(n)]
    left = [(i, (i - 1) % n) for i in range(n)]
    ahead = {0: piece}
    r = l = piece
    half = n // 2
    steps = half if n % 2 == 1 else half - 1
    for k in range(1, steps + 1):
        r = lax.ppermute(r, axis, right)
        l = lax.ppermute(l, axis, left)
        ahead[n - k] = r
        ahead[k] = l
    if n % 2 == 0 and n > 1:
        cut = piece.shape[-1] // 2
        rh = lax.ppermute(r[..., :cut], axis, right)
        lh = lax.ppermute(l[..., cut:], axis, left)
        ahead[half] = jnp.concatenate([rh, lh], axis=-1)
    stacked = jnp.stack([ahead[m] for m in range(n)])
    order = (jnp.arange(n, dtype=jnp.int32) - idx) % n
    return jnp.take(stacked, order, axis=0)


def local(tokens, cotangent, partner, combine, counts, w_gate, w_up, w_down):
    tok_rows = tokens.shape[0]
    width = tokens.shape[1]
    expert_count = lax.axis_size("expert")
    capacity = max(2, (5 * tok_rows // 4 + expert_count - 1) // expert_count)
    positions = jnp.arange(tok_rows, dtype=jnp.int32)
    valid_rows = positions < counts[0]
    weights = combine.astype(jnp.float32)
    weight_sum = weights[:, 0] + weights[:, 1]
    share_home = jnp.where(valid_rows, weights[:, 0] / weight_sum, 0.0)
    share_away = jnp.where(valid_rows, weights[:, 1] / weight_sum, 0.0)
    upstream = cotangent.astype(jnp.float32)
    q_home = (upstream * share_home[:, None]).astype(jnp.bfloat16)
    q_away = (upstream * share_away[:, None]).astype(jnp.bfloat16)
    pair = lax.all_gather(jnp.stack([w_gate[0], w_up[0]]), "replica", axis=1, tiled=False)
    down_full = ring_gather(w_down[0], "replica")
    gate_w = pair[0].reshape(-1, w_gate.shape[2])
    up_w = pair[1].reshape(-1, w_up.shape[2])
    down_w = down_full.reshape(-1, down_full.shape[2])
    target = partner[:, 0]
    onehot_rows = (target[:, None] == jnp.arange(expert_count, dtype=jnp.int32)[None, :]).astype(
        jnp.int32
    )
    rank_within = jnp.sum((jnp.cumsum(onehot_rows, axis=0) - onehot_rows) * onehot_rows, axis=1)
    destination = target * capacity + rank_within
    placing = (
        jnp.arange(expert_count * capacity, dtype=jnp.int32)[:, None] == destination[None, :]
    ).astype(jnp.bfloat16)
    send_x = (
        jnp.dot(placing, tokens, preferred_element_type=jnp.float32)
        .astype(jnp.bfloat16)
        .reshape(expert_count, capacity, width)
    )
    send_q = (
        jnp.dot(placing, q_away, preferred_element_type=jnp.float32)
        .astype(jnp.bfloat16)
        .reshape(expert_count, capacity, width)
    )
    hidden_home, grad_home = expert_backward(tokens, q_home, gate_w, up_w, down_w)
    x_there = lax.all_to_all(send_x, "expert", split_axis=0, concat_axis=0, tiled=True)
    q_there = lax.all_to_all(send_q, "expert", split_axis=0, concat_axis=0, tiled=True)
    item_count = x_there.shape[1]
    hidden_there, grad_there = expert_backward(
        x_there.reshape(-1, width), q_there.reshape(-1, width), gate_w, up_w, down_w
    )
    returned = lax.all_to_all(
        grad_there.astype(jnp.bfloat16).reshape(expert_count, item_count, width),
        "expert",
        split_axis=0,
        concat_axis=0,
        tiled=True,
    )
    returned, hidden_away, q_there = (
        returned,
        hidden_there.reshape(expert_count, item_count, -1),
        q_there,
    )
    contract = (((0,), (0,)), ((), ()))
    flat_returned = returned.reshape(expert_count * capacity, width)
    grad_away = lax.dot_general(
        placing, flat_returned, contract, preferred_element_type=jnp.float32
    )
    token_grad = (grad_home + grad_away).astype(jnp.bfloat16)
    flat_hidden = hidden_away.reshape(expert_count * capacity, -1)
    flat_q = q_there.reshape(expert_count * capacity, width)
    grad_down = lax.psum_scatter(
        (
            lax.dot_general(hidden_home, q_home, contract, preferred_element_type=jnp.float32)
            + lax.dot_general(flat_hidden, flat_q, contract, preferred_element_type=jnp.float32)
        ).astype(jnp.bfloat16),
        "replica",
        scatter_dimension=0,
        tiled=True,
    )
    return (token_grad, grad_down[None])


def solution(mesh):
    placed = (
        P(("expert", "replica"), None),
        P(("expert", "replica"), None),
        P(("expert", "replica"), None),
        P(("expert", "replica"), None),
        P(("expert", "replica")),
        P("expert", "replica", None),
        P("expert", "replica", None),
        P("expert", "replica", None),
    )
    return jax.shard_map(
        local,
        mesh=mesh,
        in_specs=placed,
        out_specs=(P(("expert", "replica"), None), P("expert", "replica", None)),
        check_vma=False,
    )
```

```python
import jax
import jax.numpy as jnp
from jax import lax
from jax.sharding import PartitionSpec as P


def against_rows(left, matrix):
    return lax.dot_general(
        left, matrix, (((1,), (1,)), ((), ())), preferred_element_type=jnp.float32
    )


def expert_backward(inputs, upstream, gate_w, up_w, down_w):
    gate_act = jnp.dot(inputs, gate_w, preferred_element_type=jnp.float32)
    up_act = jnp.dot(inputs, up_w, preferred_element_type=jnp.float32)
    sigmoid_gate = jax.nn.sigmoid(gate_act)
    swish_gate = gate_act * sigmoid_gate
    hidden = (swish_gate * up_act).astype(jnp.bfloat16)
    hidden_grad = against_rows(upstream, down_w)
    gate_grad = (
        hidden_grad * up_act * sigmoid_gate * (1.0 + gate_act * (1.0 - sigmoid_gate))
    ).astype(jnp.bfloat16)
    up_grad = (hidden_grad * swish_gate).astype(jnp.bfloat16)
    input_grad = against_rows(gate_grad, gate_w) + against_rows(up_grad, up_w)
    return (hidden, input_grad)


def ring_gather(piece, axis):
    n = lax.axis_size(axis)
    idx = lax.axis_index(axis)
    right = [(i, (i + 1) % n) for i in range(n)]
    left = [(i, (i - 1) % n) for i in range(n)]
    ahead = {0: piece}
    r = l = piece
    half = n // 2
    steps = half if n % 2 == 1 else half - 1
    for k in range(1, steps + 1):
        r = lax.ppermute(r, axis, right)
        l = lax.ppermute(l, axis, left)
        ahead[n - k] = r
        ahead[k] = l
    if n % 2 == 0 and n > 1:
        cut = piece.shape[-1] // 2
        rh = lax.ppermute(r[..., :cut], axis, right)
        lh = lax.ppermute(l[..., cut:], axis, left)
        ahead[half] = jnp.concatenate([rh, lh], axis=-1)
    stacked = jnp.stack([ahead[m] for m in range(n)])
    order = (jnp.arange(n, dtype=jnp.int32) - idx) % n
    return jnp.take(stacked, order, axis=0)


def local(tokens, cotangent, partner, combine, counts, w_gate, w_up, w_down):
    tok_rows = tokens.shape[0]
    width = tokens.shape[1]
    expert_count = lax.axis_size("expert")
    capacity = max(2, (5 * tok_rows // 4 + expert_count - 1) // expert_count)
    positions = jnp.arange(tok_rows, dtype=jnp.int32)
    valid_rows = positions < counts[0]
    weights = combine.astype(jnp.float32)
    weight_sum = weights[:, 0] + weights[:, 1]
    share_home = jnp.where(valid_rows, weights[:, 0] / weight_sum, 0.0)
    share_away = jnp.where(valid_rows, weights[:, 1] / weight_sum, 0.0)
    upstream = cotangent.astype(jnp.float32)
    q_home = (upstream * share_home[:, None]).astype(jnp.bfloat16)
    q_away = (upstream * share_away[:, None]).astype(jnp.bfloat16)
    shard_rows, hidden_units = w_gate.shape[1], w_gate.shape[2]
    down_rows, width_down = w_down.shape[1], w_down.shape[2]
    cut = width_down // 2
    packed = jnp.concatenate(
        [w_gate[0], w_up[0], w_down[0, :, :cut].reshape(-1, hidden_units)], axis=0
    )
    full = lax.all_gather(packed, "replica", axis=0, tiled=False)
    down_second = ring_gather(w_down[0, :, cut:], "replica")
    gate_w = full[:, :shard_rows].reshape(-1, hidden_units)
    up_w = full[:, shard_rows : 2 * shard_rows].reshape(-1, hidden_units)
    down_first = full[:, 2 * shard_rows :].reshape(-1, down_rows, cut)
    down_w = jnp.concatenate([down_first, down_second], axis=2).reshape(-1, width_down)
    target = partner[:, 0]
    onehot_rows = (target[:, None] == jnp.arange(expert_count, dtype=jnp.int32)[None, :]).astype(
        jnp.int32
    )
    rank_within = jnp.sum((jnp.cumsum(onehot_rows, axis=0) - onehot_rows) * onehot_rows, axis=1)
    destination = target * capacity + rank_within
    placing = (
        jnp.arange(expert_count * capacity, dtype=jnp.int32)[:, None] == destination[None, :]
    ).astype(jnp.bfloat16)
    send_x = (
        jnp.dot(placing, tokens, preferred_element_type=jnp.float32)
        .astype(jnp.bfloat16)
        .reshape(expert_count, capacity, width)
    )
    send_q = (
        jnp.dot(placing, q_away, preferred_element_type=jnp.float32)
        .astype(jnp.bfloat16)
        .reshape(expert_count, capacity, width)
    )
    x_there = lax.all_to_all(send_x, "expert", split_axis=0, concat_axis=0, tiled=True)
    q_there = lax.all_to_all(send_q, "expert", split_axis=0, concat_axis=0, tiled=True)
    item_count = x_there.shape[1]
    rows_in = jnp.concatenate([tokens, x_there.reshape(-1, width)], axis=0)
    q_in = jnp.concatenate([q_home, q_there.reshape(-1, width)], axis=0)
    hidden_all, grad_all = expert_backward(rows_in, q_in, gate_w, up_w, down_w)
    grad_home = grad_all[:tok_rows]
    grad_there = grad_all[tok_rows:]
    returned = lax.all_to_all(
        grad_there.astype(jnp.bfloat16).reshape(expert_count, item_count, width),
        "expert",
        split_axis=0,
        concat_axis=0,
        tiled=True,
    )
    contract = (((0,), (0,)), ((), ()))
    flat_returned = returned.reshape(expert_count * capacity, width)
    grad_away = lax.dot_general(
        placing, flat_returned, contract, preferred_element_type=jnp.float32
    )
    token_grad = (grad_home + grad_away).astype(jnp.bfloat16)
    grad_down = lax.psum_scatter(
        lax.dot_general(hidden_all, q_in, contract, preferred_element_type=jnp.float32).astype(
            jnp.bfloat16
        ),
        "replica",
        scatter_dimension=0,
        tiled=True,
    )
    return (token_grad, grad_down[None])


def solution(mesh):
    placed = (
        P(("expert", "replica"), None),
        P(("expert", "replica"), None),
        P(("expert", "replica"), None),
        P(("expert", "replica"), None),
        P(("expert", "replica")),
        P("expert", "replica", None),
        P("expert", "replica", None),
        P("expert", "replica", None),
    )
    return jax.shard_map(
        local,
        mesh=mesh,
        in_specs=placed,
        out_specs=(P(("expert", "replica"), None), P("expert", "replica", None)),
        check_vma=False,
    )
```
